256 devices in a mesh: vocab: 64 (over y, z, core), token: 4 (over x).
Axes of the slice: x: 4, y: 4, z: 8, core: 2. Of those that a mesh axis runs over, the one named last changes fastest.
Arguments:
- hidden: bfloat16 [32768, 4096], P(('vocab', 'token')), may hold values from -16 to 16
- cand_embed: bfloat16 [8192, 4096], P('vocab'), may hold values from -0.5 to 0.5
- freq_embed: bfloat16 [256, 4096], P('vocab'), may hold values from -0.09375 to 0.09375
- owner_order: int32 [64], replicated, may hold values from 0 to 63, each once
- cand_blocks: int32 [4096, 4], P(('vocab', 'token')), may hold values from 0 to 63, all different within a row; in each aligned block of 16 rows (0 to 15, 16 to 31, ...) at most 2 rows name the same one
- group_tokens: int32 [256, 128], P(('vocab', 'token')), may hold values from 0 to 127, each once within a row
- target_slot: int32 [32768], P(('vocab', 'token')), may hold values from 0 to 767
Outputs:
- logits: bfloat16 [32768, 768], P(('vocab', 'token'))
- loss: float32 [32768], P(('vocab', 'token'))
- grad_hidden: bfloat16 [32768, 4096], P(('vocab', 'token'))
- grad_cand: float32 [8192, 4096], P(('vocab', 'token'))
- grad_freq: float32 [256, 4096], P(('vocab', 'token'))
The draws below stay inside these ranges and needn't reach their ends.
Inputs may be any that keep to these rules, and one draw needn't show every extreme that they name: `cand_blocks`: each row names 4 different blocks. Among the 16 groups of one device no block is named by more than 2 groups, and some device reaches 2. `group_tokens`: each row lists every number below 128 once. `owner_order`: every number below 64 once.
All inputs are finite; a program needn't handle non-finite values.
Results may differ from the reference program's by a relative error of at most 0.0052.
Values may be sent and summed in bfloat16 or wider, within the bound.
No kernel may reach another device: no remote copies, remote signals or barrier semaphores. Data moves between devices by JAX's collectives and lax.ppermute only.
A program may use at most 128 MiB of HBM per device.

```python
import math
import jax
import jax.numpy as jnp
import numpy as np
from jax import lax

D = 4096
BW = 128
K = 4
GTOK = 8
PANEL = 4
G_DEV = 16
TOK_DEV = 128
TOKENS = 32768
GROUPS = 4096
CAP = 2
FREQ = 256
COLS = 768
POOL_WORDS = 8192
N_VOCAB = 64
DEVICES = 256


def draw_hidden(key, part):
    first, second = jax.random.split(key, 2)
    scales = jnp.exp(jax.random.uniform(second, (TOKENS, 1), jnp.float32, math.log(0.4), math.log(2.5)))
    values = jnp.clip(jax.random.normal(first, (TOKENS, D), jnp.float32), -6.0, 6.0) * scales
    return values.astype(jnp.bfloat16)


def draw_cand_embed(key, part):
    first, second = jax.random.split(key, 2)
    scales = jnp.exp(jax.random.uniform(second, (POOL_WORDS, 1), jnp.float32, math.log(0.4), math.log(2.5)))
    base = jnp.clip(jax.random.normal(first, (POOL_WORDS, D), jnp.float32), -6.0, 6.0)
    values = jnp.clip(base * scales * D ** (-0.5), -0.5, 0.5)
    return values.astype(jnp.bfloat16)


def plant(entries, key, smallest, largest):
    place = [jax.random.randint(jax.random.fold_in(key, axis), (), 0, length) for axis, length in enumerate(entries.shape)]
    main_axis = entries.shape.index(max(entries.shape))
    neighbour = place[:main_axis] + [(place[main_axis] + 1) % entries.shape[main_axis]] + place[main_axis + 1:]
    return entries.at[tuple(place)].set(smallest).at[tuple(neighbour)].set(largest)


def steps_of(own_key, shape, cuts, smallest, top_value):
    def one(dim, shards_of):
        heights = jax.random.uniform(jax.random.fold_in(jax.random.fold_in(own_key, 6), dim), (shards_of,), jnp.float32, smallest / len(cuts), top_value / len(cuts))
        return jnp.repeat(jnp.exp(heights), shape[dim] // shards_of).reshape((-1,) + (1,) * (len(shape) - dim - 1))

    level = one(*cuts[0])
    for cut in cuts[1:]:
        level = level * one(*cut)
    return level


def routed_block(own_key, own, number, rows, number_of, top, limit, skew):
    order = jax.random.permutation(own_key, number_of)
    packed, ordinary = load_shares(number_of, rows * top, limit, skew, True), load_shares(number_of, rows * top, limit, skew, False)
    places = jnp.arange(number_of)

    def named(tallies, rotation):
        used = int((tallies > 0).sum())
        fixed = max(1, used // 4)
        passed = fixed + (places - fixed + rotation * (used - fixed)) % max(1, number_of - fixed)
        return jnp.zeros((number_of,), jnp.int32).at[order[jnp.where(places < fixed, places, passed)]].set(jnp.asarray(tallies, jnp.int32))

    tallies = jnp.where(number % 4 == 0, named(packed, number // 4), named(ordinary, number - number // 4 - 1))
    mixed = jax.random.permutation(jax.random.fold_in(own, 3), number_of)
    giver, sink = mixed[0:number_of // 2 * 2:2], mixed[1:number_of // 2 * 2:2]
    margin = jnp.minimum(tallies[giver] - 1, limit - tallies[sink]) // 2
    margin = jnp.where((giver == order[0]) | (sink == order[0]) | (tallies[sink] == 0), 0, jnp.maximum(margin, 0))
    passed = jax.random.randint(jax.random.fold_in(own, 4), (number_of // 2,), 0, 1 << 20) % (margin + 1)
    tallies = tallies.at[giver].add(-passed).at[sink].add(passed)
    labels = jnp.searchsorted(jnp.cumsum(tallies), jnp.arange(rows * top), side="right").astype(jnp.int32)
    table = labels.reshape(top, rows).T
    table = table[jax.random.permutation(jax.random.fold_in(own, 1), rows)]
    rotation = jax.random.randint(jax.random.fold_in(own, 2), (rows, 1), 0, top)
    return jnp.take_along_axis(table, (jnp.arange(top)[None, :] + rotation) % top, axis=1)


def load_shares(number_of, total, most, slope, full):
    portions = [(1 << 20) // math.isqrt(grade ** slope) + 1 for grade in range(1, number_of + 1)]
    largest = most if full else min(most, max(-(-total // number_of), total * portions[0] // sum(portions)))
    least = 1 if total - largest >= number_of - 1 else 0
    counts, surplus = [largest] + [least] * (number_of - 1), total - largest - least * (number_of - 1)
    while surplus > 0:
        movable = [i for i in range(1, number_of) if counts[i] < largest] or [i for i in range(1, number_of) if counts[i] < most]
        pool, left = sum([portions[i] for i in movable]), surplus
        for i in movable:
            extra = min(most - counts[i], max(1, left * portions[i] // pool), surplus)
            counts[i] = counts[i] + extra
            surplus = surplus - extra
    return np.array(counts)


def noise(key, dims, scale, most, cuts=(), held_as=jnp.bfloat16):
    level = steps_of(key, dims, cuts, -0.22, 0.18) if cuts else 1.0
    drawn = jax.random.normal(key, dims, jnp.float32) * scale * level
    return jnp.minimum(jnp.maximum(drawn, -most), most).astype(held_as)


def setup_inputs(seed: int = 0) -> dict:
    splits = jax.random.split(jax.random.key(seed), 8)
    hidden = draw_hidden(jax.random.fold_in(splits[7], 71), 0)
    cand_embed = draw_cand_embed(jax.random.fold_in(splits[7], 71), 0)
    freq_embed = noise(splits[2], (FREQ, D), D ** -0.5, 0.09375, ((0, 64),))
    owner_order = jax.random.permutation(splits[3], N_VOCAB).astype(jnp.int32)
    cand_blocks_keys = jax.random.split(jax.random.fold_in(splits[4], 1), GROUPS // G_DEV)
    cand_blocks_turns = jax.random.permutation(jax.random.fold_in(splits[4], 3), GROUPS // G_DEV)
    cand_blocks = jax.vmap(lambda own, number: routed_block(jax.random.fold_in(splits[4], 2), own, number, G_DEV, N_VOCAB, K, CAP, 2))(cand_blocks_keys, cand_blocks_turns).reshape((GROUPS, K))
    group_tokens = jax.vmap(lambda own: jax.random.permutation(own, TOK_DEV))(jax.random.split(splits[5], DEVICES)).reshape((DEVICES, TOK_DEV)).astype(jnp.int32)
    target_slot = plant(jax.random.randint(splits[6], (TOKENS,), 0, COLS), jax.random.fold_in(splits[6], 1), 0, COLS - 1).astype(jnp.int32)
    return {"hidden": hidden, "cand_embed": cand_embed, "freq_embed": freq_embed, "owner_order": owner_order, "cand_blocks": cand_blocks, "group_tokens": group_tokens, "target_slot": target_slot}


def reference(hidden, cand_embed, freq_embed, owner_order, cand_blocks, group_tokens, target_slot):
    freq_table = freq_embed.reshape(N_VOCAB, PANEL, D)[owner_order].reshape(FREQ, D)
    freq_wide = freq_table.astype(jnp.float32)
    block_table = cand_embed.reshape(N_VOCAB, BW, D)
    columns = jnp.arange(COLS, dtype=jnp.int32)
    positions = jnp.arange(TOK_DEV, dtype=jnp.int32)

    def one_device(carry, inputs):
        cand_grad, freq_grad = carry
        device_rows, listing, device_targets, device_blocks = inputs
        gathered = device_rows[listing].reshape(G_DEV, GTOK, D).astype(jnp.float32)
        wanted = device_targets[listing].reshape(G_DEV, GTOK)
        chosen = block_table[device_blocks].astype(jnp.float32)
        freq_scores = jnp.einsum("gtd,fd->gtf", gathered, freq_wide)
        cand_scores = jnp.einsum("gtd,gkwd->gtkw", gathered, chosen).reshape(G_DEV, GTOK, K * BW)
        scores = jnp.concatenate([freq_scores, cand_scores], axis=-1)
        row_top = jnp.max(scores, axis=-1)
        exponentials = jnp.exp(scores - row_top[..., None])
        total = jnp.sum(exponentials, axis=-1)
        target_hot = (wanted[..., None] == columns).astype(jnp.float32)
        token_loss = jnp.log(total) + row_top - jnp.sum(target_hot * scores, axis=-1)
        prob_short = (exponentials * (1.0 / total)[..., None] - target_hot).astype(jnp.bfloat16)
        probgrad = lax.optimization_barrier(prob_short).astype(jnp.float32)
        prob_freq = probgrad[..., :FREQ]
        prob_cand = probgrad[..., FREQ:].reshape(G_DEV, GTOK, K, BW)
        part_short = jnp.einsum("gtkw,gkwd->gtkd", prob_cand, chosen).astype(jnp.bfloat16)
        block_part = lax.optimization_barrier(part_short).astype(jnp.float32)
        grad_rows = jnp.einsum("gtf,fd->gtd", prob_freq, freq_wide) + jnp.sum(block_part, axis=2)
        block_term = jnp.einsum("gtkw,gtd->gkwd", prob_cand, gathered).reshape(G_DEV * K, BW, D)
        cand_grad = cand_grad.at[device_blocks.reshape(G_DEV * K)].add(block_term)
        freq_grad = freq_grad + jnp.einsum("gtf,gtd->fd", prob_freq, gathered)
        undo = jnp.zeros((TOK_DEV,), jnp.int32).at[listing].set(positions)
        device_logits = scores.reshape(TOK_DEV, COLS).astype(jnp.bfloat16)[undo]
        device_loss = token_loss.reshape(TOK_DEV)[undo]
        device_grad = grad_rows.reshape(TOK_DEV, D).astype(jnp.bfloat16)[undo]
        return (cand_grad, freq_grad), (device_logits, device_loss, device_grad)

    start_carry = (jnp.zeros((N_VOCAB, BW, D), jnp.float32), jnp.zeros((FREQ, D), jnp.float32))
    inputs = (hidden.reshape(DEVICES, TOK_DEV, D), group_tokens,
              target_slot.reshape(DEVICES, TOK_DEV), cand_blocks.reshape(DEVICES, G_DEV, K))
    (cand_grad, freq_grad), (all_logits, all_loss, all_grad) = lax.scan(one_device, start_carry, inputs)
    grad_freq = jnp.zeros((N_VOCAB, PANEL, D), jnp.float32).at[owner_order].set(
        freq_grad.reshape(N_VOCAB, PANEL, D)).reshape(FREQ, D)
    return (all_logits.reshape(TOKENS, COLS), all_loss.reshape(TOKENS), all_grad.reshape(TOKENS, D),
            cand_grad.reshape(POOL_WORDS, D), grad_freq)
```

```python
import jax
import jax.numpy as jnp
from jax import lax
from jax.sharding import PartitionSpec as P

D = 4096
BW = 128
K = 4
GTOK = 8
PANEL = 4
G_DEV = 16


def per_device(hidden, cand_embed, freq_embed, owner_order, cand_blocks, group_tokens, target_slot):
    owners_count = lax.axis_size("vocab")
    token_total = hidden.shape[0]
    freq_count = owners_count * PANEL
    capacity = 2 * G_DEV * K // owners_count
    slot_count = owners_count * capacity
    requests = G_DEV * K
    listing = group_tokens[0]
    grouped = hidden[listing]
    targets = target_slot[listing]
    panels = lax.all_gather(freq_embed, "vocab", axis=0, tiled=True)
    freq_table = panels.reshape(owners_count, PANEL, D)[owner_order].reshape(freq_count, D)
    owner_of = cand_blocks.reshape(requests)
    owner_hot = (owner_of[:, None] == jnp.arange(owners_count, dtype=jnp.int32)[None, :]).astype(
        jnp.int32
    )
    ranking = jnp.sum(jnp.cumsum(owner_hot, axis=0) * owner_hot, axis=1) - 1
    landing = owner_of * capacity + ranking
    placed = (landing[None, :] == jnp.arange(slot_count, dtype=jnp.int32)[:, None]).astype(
        jnp.int32
    )
    occupied = jnp.sum(placed, axis=1)
    request_of = jnp.sum(placed * jnp.arange(requests, dtype=jnp.int32)[None, :], axis=1)
    group_of = request_of // K
    block_rank = request_of % K
    group_rows = grouped.reshape(G_DEV, GTOK, D)
    slot_mask = occupied.astype(jnp.bfloat16)[:, None, None]
    send_rows = (group_rows[group_of] * slot_mask).reshape(owners_count, capacity, GTOK, D)
    group_targets = targets.reshape(G_DEV, GTOK)
    column = group_targets[group_of] - freq_count - block_rank[:, None] * BW
    inside = (column >= 0) & (column < BW) & (occupied[:, None] > 0)
    send_column = jnp.where(inside, column, -1).reshape(owners_count, capacity, GTOK)
    got_rows = lax.all_to_all(send_rows, "vocab", split_axis=0, concat_axis=0, tiled=True)
    scores_here = jnp.einsum(
        "scqd,wd->scqw", got_rows, cand_embed, preferred_element_type=jnp.float32
    )
    scores_home = lax.all_to_all(scores_here, "vocab", split_axis=0, concat_axis=0, tiled=True)
    returned = scores_home.reshape(slot_count, GTOK, BW)[landing]
    cand_scores = (
        returned.reshape(G_DEV, K, GTOK, BW).transpose(0, 2, 1, 3).reshape(token_total, K * BW)
    )
    freq_scores = jnp.einsum("td,fd->tf", grouped, freq_table, preferred_element_type=jnp.float32)
    all_scores = jnp.concatenate([freq_scores, cand_scores], axis=1)
    row_top = jnp.max(all_scores, axis=1)
    exponentials = jnp.exp(all_scores - row_top[:, None])
    total = jnp.sum(exponentials, axis=1)
    inverse_total = 1.0 / total
    columns = jnp.arange(all_scores.shape[1], dtype=jnp.int32)
    target_hot = (targets[:, None] == columns[None, :]).astype(jnp.float32)
    token_loss = jnp.log(total) + row_top - jnp.sum(target_hot * all_scores, axis=1)
    prob_freq = (
        exponentials[:, :freq_count] * inverse_total[:, None] - target_hot[:, :freq_count]
    ).astype(jnp.bfloat16)
    slot_live = occupied[:, None].astype(jnp.float32)
    send_scale = (inverse_total.reshape(G_DEV, GTOK)[group_of] * slot_live).reshape(
        owners_count, capacity, GTOK
    )
    send_top = (row_top.reshape(G_DEV, GTOK)[group_of] * slot_live).reshape(
        owners_count, capacity, GTOK
    )
    send_stats = jnp.stack([send_scale, send_top, send_column.astype(jnp.float32)], axis=-1)
    got_stats = lax.all_to_all(send_stats, "vocab", split_axis=0, concat_axis=0, tiled=True)
    got_scale, got_top = got_stats[..., 0], got_stats[..., 1]
    got_column = got_stats[..., 2].astype(jnp.int32)
    word_index = jnp.arange(BW, dtype=jnp.int32)
    is_target = (got_column[..., None] == word_index).astype(jnp.float32)
    prob_here = (
        jnp.exp(scores_here - got_top[..., None]) * got_scale[..., None] - is_target
    ).astype(jnp.bfloat16)
    hidden_part = jnp.einsum(
        "scqw,wd->scqd", prob_here, cand_embed, preferred_element_type=jnp.float32
    ).astype(jnp.bfloat16)
    parts_home = lax.all_to_all(hidden_part, "vocab", split_axis=0, concat_axis=0, tiled=True)
    window = prob_here
    grad_cand = lax.psum_scatter(
        jnp.einsum("scqw,scqd->wd", window, got_rows, preferred_element_type=jnp.float32),
        "token",
        scatter_dimension=0,
        tiled=True,
    )
    part_rows = parts_home.reshape(slot_count, GTOK, D)[landing].reshape(G_DEV, K, GTOK, D)
    freq_part = jnp.dot(prob_freq, freq_table, preferred_element_type=jnp.float32)
    grad_rows = freq_part + jnp.sum(part_rows, axis=1, dtype=jnp.float32).reshape(token_total, D)
    position_of = (
        jnp.zeros((owners_count,), jnp.int32)
        .at[owner_order]
        .set(jnp.arange(owners_count, dtype=jnp.int32))
    )
    embed_columns = (
        position_of[:, None] * PANEL + jnp.arange(PANEL, dtype=jnp.int32)[None, :]
    ).reshape(freq_count)
    prob_embed = prob_freq[:, embed_columns]
    window = prob_embed
    token_count = lax.axis_size("token")
    freq_partial = jnp.einsum("tf,td->fd", window, grouped, preferred_element_type=jnp.float32)
    freq_partial = freq_partial.reshape(freq_count // token_count, token_count, D).transpose(1, 0, 2)
    freq_partial = lax.psum_scatter(freq_partial, "token", scatter_dimension=0, tiled=True)
    grad_freq = lax.psum_scatter(
        freq_partial.reshape(freq_count // token_count, D), "vocab", scatter_dimension=0, tiled=True
    )
    undo = (
        jnp.zeros((token_total,), jnp.int32)
        .at[listing]
        .set(jnp.arange(token_total, dtype=jnp.int32))
    )
    logits = all_scores.astype(jnp.bfloat16)[undo]
    loss = token_loss[undo]
    grad_hidden = grad_rows.astype(jnp.bfloat16)[undo]
    return (logits, loss, grad_hidden, grad_cand, grad_freq)


def solution(mesh):
    in_specs = (
        P(("vocab", "token"), None),
        P("vocab", None),
        P("vocab", None),
        P(),
        P(("vocab", "token"), None),
        P(("vocab", "token"), None),
        P(("vocab", "token")),
    )
    out_specs = (
        P(("vocab", "token"), None),
        P(("vocab", "token")),
        P(("vocab", "token"), None),
        P(("vocab", "token"), None),
        P(("vocab", "token"), None),
    )
    return jax.shard_map(
        per_device, mesh=mesh, in_specs=in_specs, out_specs=out_specs, check_vma=False
    )
```

```python
import jax
import jax.numpy as jnp
from jax import lax
from jax.sharding import PartitionSpec as P

D = 4096
BW = 128
K = 4
GTOK = 8
PANEL = 4
G_DEV = 16


def per_device(hidden, cand_embed, freq_embed, owner_order, cand_blocks, group_tokens, target_slot):
    owners_count = lax.axis_size("vocab")
    token_total = hidden.shape[0]
    freq_count = owners_count * PANEL
    capacity = 2 * G_DEV * K // owners_count
    slot_count = owners_count * capacity
    requests = G_DEV * K
    listing = group_tokens[0]
    grouped = hidden[listing]
    targets = target_slot[listing]
    panels = lax.all_gather(freq_embed, "vocab", axis=0, tiled=True)
    freq_table = panels.reshape(owners_count, PANEL, D)[owner_order].reshape(freq_count, D)
    owner_of = cand_blocks.reshape(requests)
    owner_hot = (owner_of[:, None] == jnp.arange(owners_count, dtype=jnp.int32)[None, :]).astype(
        jnp.int32
    )
    ranking = jnp.sum(jnp.cumsum(owner_hot, axis=0) * owner_hot, axis=1) - 1
    landing = owner_of * capacity + ranking
    placed = (landing[None, :] == jnp.arange(slot_count, dtype=jnp.int32)[:, None]).astype(
        jnp.int32
    )
    occupied = jnp.sum(placed, axis=1)
    request_of = jnp.sum(placed * jnp.arange(requests, dtype=jnp.int32)[None, :], axis=1)
    group_of = request_of // K
    block_rank = request_of % K
    send_rows = hidden[listing.reshape(G_DEV, GTOK)[group_of]].reshape(owners_count, capacity, GTOK, D)
    group_targets = targets.reshape(G_DEV, GTOK)
    column = group_targets[group_of] - freq_count - block_rank[:, None] * BW
    inside = (column >= 0) & (column < BW) & (occupied[:, None] > 0)
    send_column = jnp.where(inside, column, -1).reshape(owners_count, capacity, GTOK)
    got_rows = lax.all_to_all(send_rows, "vocab", split_axis=0, concat_axis=0, tiled=True)
    scores_here = jnp.einsum(
        "scqd,wd->scqw", got_rows, cand_embed, preferred_element_type=jnp.float32
    )
    scores_home = lax.all_to_all(scores_here, "vocab", split_axis=0, concat_axis=0, tiled=True)
    returned = scores_home.reshape(slot_count, GTOK, BW)[landing]
    cand_scores = (
        returned.reshape(G_DEV, K, GTOK, BW).transpose(0, 2, 1, 3).reshape(token_total, K * BW)
    )
    freq_scores = jnp.einsum("td,fd->tf", grouped, freq_table, preferred_element_type=jnp.float32)
    all_scores = jnp.concatenate([freq_scores, cand_scores], axis=1)
    row_top = jnp.max(all_scores, axis=1)
    exponentials = jnp.exp(all_scores - row_top[:, None])
    total = jnp.sum(exponentials, axis=1)
    inverse_total = 1.0 / total
    columns = jnp.arange(all_scores.shape[1], dtype=jnp.int32)
    target_hot = (targets[:, None] == columns[None, :]).astype(jnp.float32)
    token_loss = jnp.log(total) + row_top - jnp.sum(target_hot * all_scores, axis=1)
    prob_freq = (
        exponentials[:, :freq_count] * inverse_total[:, None] - target_hot[:, :freq_count]
    ).astype(jnp.bfloat16)
    slot_live = occupied[:, None].astype(jnp.float32)
    send_scale = (inverse_total.reshape(G_DEV, GTOK)[group_of] * slot_live).reshape(
        owners_count, capacity, GTOK
    )
    send_top = (row_top.reshape(G_DEV, GTOK)[group_of] * slot_live).reshape(
        owners_count, capacity, GTOK
    )
    send_stats = jnp.stack([send_scale, send_top, send_column.astype(jnp.float32)], axis=-1)
    got_stats = lax.all_to_all(send_stats, "vocab", split_axis=0, concat_axis=0, tiled=True)
    got_scale, got_top = got_stats[..., 0], got_stats[..., 1]
    got_column = got_stats[..., 2].astype(jnp.int32)
    word_index = jnp.arange(BW, dtype=jnp.int32)
    is_target = (got_column[..., None] == word_index).astype(jnp.float32)
    live_here = got_scale[..., None] > 0
    prob_here = (
        jnp.where(live_here, jnp.exp(scores_here - got_top[..., None]) * got_scale[..., None], 0.0)
        - is_target
    ).astype(jnp.bfloat16)
    hidden_part = jnp.einsum(
        "scqw,wd->scqd", prob_here, cand_embed, preferred_element_type=jnp.float32
    ).astype(jnp.bfloat16)
    parts_home = lax.all_to_all(hidden_part, "vocab", split_axis=0, concat_axis=0, tiled=True)
    window = prob_here
    grad_cand = lax.psum_scatter(
        jnp.einsum("scqw,scqd->wd", window, got_rows, preferred_element_type=jnp.float32),
        "token",
        scatter_dimension=0,
        tiled=True,
    )
    part_rows = parts_home.reshape(slot_count, GTOK, D)[landing].reshape(G_DEV, K, GTOK, D)
    freq_part = jnp.dot(prob_freq, freq_table, preferred_element_type=jnp.float32)
    grad_rows = freq_part + jnp.sum(part_rows, axis=1, dtype=jnp.float32).reshape(token_total, D)
    position_of = (
        jnp.zeros((owners_count,), jnp.int32)
        .at[owner_order]
        .set(jnp.arange(owners_count, dtype=jnp.int32))
    )
    embed_columns = (
        position_of[:, None] * PANEL + jnp.arange(PANEL, dtype=jnp.int32)[None, :]
    ).reshape(freq_count)
    prob_embed = prob_freq[:, embed_columns]
    window = prob_embed
    token_count = lax.axis_size("token")
    freq_partial = jnp.einsum("tf,td->fd", window, grouped, preferred_element_type=jnp.float32)
    freq_partial = freq_partial.reshape(freq_count // token_count, token_count, D).transpose(1, 0, 2)
    freq_partial = lax.psum_scatter(freq_partial, "token", scatter_dimension=0, tiled=True)
    freq_pieces = lax.all_to_all(
        freq_partial.reshape(freq_count // token_count, D), "vocab", split_axis=0, concat_axis=0, tiled=True
    )
    grad_freq = jnp.sum(freq_pieces, axis=0, keepdims=True)
    undo = (
        jnp.zeros((token_total,), jnp.int32)
        .at[listing]
        .set(jnp.arange(token_total, dtype=jnp.int32))
    )
    logits = all_scores.astype(jnp.bfloat16)[undo]
    loss = token_loss[undo]
    grad_hidden = grad_rows.astype(jnp.bfloat16)[undo]
    return (logits, loss, grad_hidden, grad_cand, grad_freq)


def solution(mesh):
    in_specs = (
        P(("vocab", "token"), None),
        P("vocab", None),
        P("vocab", None),
        P(),
        P(("vocab", "token"), None),
        P(("vocab", "token"), None),
        P(("vocab", "token")),
    )
    out_specs = (
        P(("vocab", "token"), None),
        P(("vocab", "token")),
        P(("vocab", "token"), None),
        P(("vocab", "token"), None),
        P(("vocab", "token"), None),
    )
    return jax.shard_map(
        per_device, mesh=mesh, in_specs=in_specs, out_specs=out_specs, check_vma=False
    )
```

```python
import jax
import jax.numpy as jnp
from jax import lax
from jax.sharding import PartitionSpec as P

D = 4096
BW = 128
K = 4
GTOK = 8
PANEL = 4
G_DEV = 16


def halving_sum(rows, axis):
    count = lax.axis_size(axis)
    depth = count.bit_length() - 1
    me = lax.axis_index(axis)
    pieces = rows.reshape((2,) * depth + rows.shape[1:])
    bits = list(range(depth - 1, -1, -1))
    order = [0, 1, 4, 2, 5, 3] if depth == 6 else list(range(depth))
    for bit in order:
        place = bits.index(bit)
        mine = (me >> bit) & 1
        keep = lax.dynamic_index_in_dim(pieces, mine, axis=place, keepdims=False)
        give = lax.dynamic_index_in_dim(pieces, 1 - mine, axis=place, keepdims=False)
        pairs = [(i, i ^ (1 << bit)) for i in range(count)]
        pieces = keep + lax.ppermute(give, axis, pairs)
        bits.remove(bit)
    return pieces.reshape((1,) + rows.shape[1:])


def per_device_body(hidden, cand_embed, freq_embed, owner_order, cand_blocks, group_tokens, target_slot):
    owners_count = lax.axis_size("vocab")
    token_total = hidden.shape[0]
    freq_count = owners_count * PANEL
    capacity = 2 * G_DEV * K // owners_count
    slot_count = owners_count * capacity
    requests = G_DEV * K
    listing = group_tokens[0]
    grouped = hidden[listing]
    targets = target_slot[listing]
    panels = lax.all_gather(freq_embed, "vocab", axis=0, tiled=True)
    freq_table = panels.reshape(owners_count, PANEL, D)[owner_order].reshape(freq_count, D)
    owner_of = cand_blocks.reshape(requests)
    owner_hot = (owner_of[:, None] == jnp.arange(owners_count, dtype=jnp.int32)[None, :]).astype(
        jnp.int32
    )
    ranking = jnp.sum(jnp.cumsum(owner_hot, axis=0) * owner_hot, axis=1) - 1
    landing = owner_of * capacity + ranking
    placed = (landing[None, :] == jnp.arange(slot_count, dtype=jnp.int32)[:, None]).astype(
        jnp.int32
    )
    occupied = jnp.sum(placed, axis=1)
    request_of = jnp.sum(placed * jnp.arange(requests, dtype=jnp.int32)[None, :], axis=1)
    group_of = request_of // K
    block_rank = request_of % K
    send_rows = hidden[listing.reshape(G_DEV, GTOK)[group_of]].reshape(owners_count, capacity, GTOK, D)
    group_targets = targets.reshape(G_DEV, GTOK)
    column = group_targets[group_of] - freq_count - block_rank[:, None] * BW
    inside = (column >= 0) & (column < BW) & (occupied[:, None] > 0)
    send_column = jnp.where(inside, column, -1).reshape(owners_count, capacity, GTOK)
    got_rows = lax.all_to_all(send_rows, "vocab", split_axis=0, concat_axis=0, tiled=True)
    scores_here = jnp.einsum(
        "scqd,wd->scqw", got_rows, cand_embed, preferred_element_type=jnp.float32
    )
    scores_home = lax.all_to_all(scores_here, "vocab", split_axis=0, concat_axis=0, tiled=True)
    returned = scores_home.reshape(slot_count, GTOK, BW)[landing]
    cand_scores = (
        returned.reshape(G_DEV, K, GTOK, BW).transpose(0, 2, 1, 3).reshape(token_total, K * BW)
    )
    freq_scores = jnp.einsum("td,fd->tf", grouped, freq_table, preferred_element_type=jnp.float32)
    all_scores = jnp.concatenate([freq_scores, cand_scores], axis=1)
    row_top = jnp.max(all_scores, axis=1)
    exponentials = jnp.exp(all_scores - row_top[:, None])
    total = jnp.sum(exponentials, axis=1)
    inverse_total = 1.0 / total
    columns = jnp.arange(all_scores.shape[1], dtype=jnp.int32)
    target_hot = (targets[:, None] == columns[None, :]).astype(jnp.float32)
    token_loss = jnp.log(total) + row_top - jnp.sum(target_hot * all_scores, axis=1)
    prob_freq = (
        exponentials[:, :freq_count] * inverse_total[:, None] - target_hot[:, :freq_count]
    ).astype(jnp.bfloat16)
    slot_live = occupied[:, None].astype(jnp.float32)
    send_scale = (inverse_total.reshape(G_DEV, GTOK)[group_of] * slot_live).reshape(
        owners_count, capacity, GTOK
    )
    send_top = (row_top.reshape(G_DEV, GTOK)[group_of] * slot_live).reshape(
        owners_count, capacity, GTOK
    )
    send_stats = jnp.stack([send_scale, send_top, send_column.astype(jnp.float32)], axis=-1)
    got_stats = lax.all_to_all(send_stats, "vocab", split_axis=0, concat_axis=0, tiled=True)
    got_scale, got_top = got_stats[..., 0], got_stats[..., 1]
    got_column = got_stats[..., 2].astype(jnp.int32)
    word_index = jnp.arange(BW, dtype=jnp.int32)
    is_target = (got_column[..., None] == word_index).astype(jnp.float32)
    live_here = got_scale[..., None] > 0
    prob_here = (
        jnp.where(live_here, jnp.exp(scores_here - got_top[..., None]) * got_scale[..., None], 0.0)
        - is_target
    ).astype(jnp.bfloat16)
    hidden_part = jnp.einsum(
        "scqw,wd->scqd", prob_here, cand_embed, preferred_element_type=jnp.float32
    ).astype(jnp.bfloat16)
    hidden_part, prob_late = lax.optimization_barrier((hidden_part, prob_freq))
    parts_home = lax.all_to_all(hidden_part, "vocab", split_axis=0, concat_axis=0, tiled=True)
    window = prob_here
    grad_cand = lax.psum_scatter(
        jnp.einsum("scqw,scqd->wd", window, got_rows, preferred_element_type=jnp.float32),
        "token",
        scatter_dimension=0,
        tiled=True,
    )
    part_rows = parts_home.reshape(slot_count, GTOK, D)[landing].reshape(G_DEV, K, GTOK, D)
    freq_part = jnp.dot(prob_freq, freq_table, preferred_element_type=jnp.float32)
    grad_rows = freq_part + jnp.sum(part_rows, axis=1, dtype=jnp.float32).reshape(token_total, D)
    position_of = (
        jnp.zeros((owners_count,), jnp.int32)
        .at[owner_order]
        .set(jnp.arange(owners_count, dtype=jnp.int32))
    )
    embed_columns = (
        position_of[:, None] * PANEL + jnp.arange(PANEL, dtype=jnp.int32)[None, :]
    ).reshape(freq_count)
    token_count = lax.axis_size("token")
    embed_columns = (
        embed_columns.reshape(freq_count // token_count, token_count).T.reshape(freq_count)
    )
    prob_embed = prob_late[:, embed_columns]
    window = prob_embed
    freq_partial = jnp.einsum("tf,td->fd", window, grouped, preferred_element_type=jnp.float32)
    freq_partial = freq_partial.reshape(token_count, freq_count // token_count, D)
    freq_partial = lax.psum_scatter(freq_partial, "token", scatter_dimension=0, tiled=True)
    grad_freq = halving_sum(freq_partial.reshape(owners_count, D), "vocab")
    undo = (
        jnp.zeros((token_total,), jnp.int32)
        .at[listing]
        .set(jnp.arange(token_total, dtype=jnp.int32))
    )
    logits = all_scores.astype(jnp.bfloat16)[undo]
    loss = token_loss[undo]
    grad_hidden = grad_rows.astype(jnp.bfloat16)[undo]
    return (logits, loss, grad_hidden, grad_cand, grad_freq)


def solution(mesh):
    in_specs = (
        P(("vocab", "token"), None),
        P("vocab", None),
        P("vocab", None),
        P(),
        P(("vocab", "token"), None),
        P(("vocab", "token"), None),
        P(("vocab", "token")),
    )
    out_specs = (
        P(("vocab", "token"), None),
        P(("vocab", "token")),
        P(("vocab", "token"), None),
        P(("vocab", "token"), None),
        P(("vocab", "token"), None),
    )
    return jax.shard_map(
        per_device_body, mesh=mesh, in_specs=in_specs, out_specs=out_specs, check_vma=False
    )
```

```python
import jax
import jax.numpy as jnp
from jax import lax
from jax.sharding import PartitionSpec as P

D = 4096
BW = 128
K = 4
GTOK = 8
PANEL = 4
G_DEV = 16


def halving_sum(rows, axis):
    count = lax.axis_size(axis)
    depth = count.bit_length() - 1
    me = lax.axis_index(axis)
    pieces = rows.reshape((2,) * depth + rows.shape[1:])
    bits = list(range(depth - 1, -1, -1))
    order = [0, 4, 5, 1, 2, 3] if depth == 6 else list(range(depth))
    for bit in order:
        place = bits.index(bit)
        mine = (me >> bit) & 1
        keep = lax.dynamic_index_in_dim(pieces, mine, axis=place, keepdims=False)
        give = lax.dynamic_index_in_dim(pieces, 1 - mine, axis=place, keepdims=False)
        pairs = [(i, i ^ (1 << bit)) for i in range(count)]
        pieces = keep + lax.ppermute(give, axis, pairs)
        bits.remove(bit)
    return pieces.reshape((1,) + rows.shape[1:])


def per_device_body(hidden, cand_embed, freq_embed, owner_order, cand_blocks, group_tokens, target_slot):
    owners_count = lax.axis_size("vocab")
    token_total = hidden.shape[0]
    freq_count = owners_count * PANEL
    capacity = 2 * G_DEV * K // owners_count
    slot_count = owners_count * capacity
    requests = G_DEV * K
    listing = group_tokens[0]
    grouped = hidden[listing]
    targets = target_slot[listing]
    token_count = lax.axis_size("token")
    my_row = lax.dynamic_index_in_dim(freq_embed, lax.axis_index("token"), axis=0, keepdims=True)
    panel_rows = lax.all_gather(my_row, "vocab", axis=0, tiled=True)
    token_me = lax.axis_index("token")
    panels = [panel_rows]
    for shift in range(1, token_count):
        pairs = [(i, (i + shift) % token_count) for i in range(token_count)]
        panels.append(lax.ppermute(panel_rows, "token", pairs))
    panels = jnp.concatenate(panels, axis=0)
    source_shift = (token_me - jnp.arange(PANEL, dtype=jnp.int32)) % token_count
    table_rows = (source_shift[None, :] * owners_count + owner_order[:, None]).reshape(freq_count)
    freq_table = panels[table_rows]
    owner_of = cand_blocks.reshape(requests)
    owner_hot = (owner_of[:, None] == jnp.arange(owners_count, dtype=jnp.int32)[None, :]).astype(
        jnp.int32
    )
    ranking = jnp.sum(jnp.cumsum(owner_hot, axis=0) * owner_hot, axis=1) - 1
    landing = owner_of * capacity + ranking
    placed = (landing[None, :] == jnp.arange(slot_count, dtype=jnp.int32)[:, None]).astype(
        jnp.int32
    )
    occupied = jnp.sum(placed, axis=1)
    request_of = jnp.sum(placed * jnp.arange(requests, dtype=jnp.int32)[None, :], axis=1)
    group_of = request_of // K
    block_rank = request_of % K
    send_rows = hidden[listing.reshape(G_DEV, GTOK)[group_of]].reshape(owners_count, capacity, GTOK, D)
    group_targets = targets.reshape(G_DEV, GTOK)
    column = group_targets[group_of] - freq_count - block_rank[:, None] * BW
    inside = (column >= 0) & (column < BW) & (occupied[:, None] > 0)
    send_column = jnp.where(inside, column, -1).reshape(owners_count, capacity, GTOK)
    got_rows = lax.all_to_all(send_rows, "vocab", split_axis=0, concat_axis=0, tiled=True)
    scores_here = jnp.einsum(
        "scqd,wd->scqw", got_rows, cand_embed, preferred_element_type=jnp.float32
    )
    scores_home = lax.all_to_all(scores_here, "vocab", split_axis=0, concat_axis=0, tiled=True)
    returned = scores_home.reshape(slot_count, GTOK, BW)[landing]
    cand_scores = (
        returned.reshape(G_DEV, K, GTOK, BW).transpose(0, 2, 1, 3).reshape(token_total, K * BW)
    )
    freq_scores = jnp.einsum("td,fd->tf", grouped, freq_table, preferred_element_type=jnp.float32)
    all_scores = jnp.concatenate([freq_scores, cand_scores], axis=1)
    row_top = jnp.max(all_scores, axis=1)
    exponentials = jnp.exp(all_scores - row_top[:, None])
    total = jnp.sum(exponentials, axis=1)
    inverse_total = 1.0 / total
    columns = jnp.arange(all_scores.shape[1], dtype=jnp.int32)
    target_hot = (targets[:, None] == columns[None, :]).astype(jnp.float32)
    token_loss = jnp.log(total) + row_top - jnp.sum(target_hot * all_scores, axis=1)
    prob_freq = (
        exponentials[:, :freq_count] * inverse_total[:, None] - target_hot[:, :freq_count]
    ).astype(jnp.bfloat16)
    slot_live = occupied[:, None].astype(jnp.float32)
    send_scale = (inverse_total.reshape(G_DEV, GTOK)[group_of] * slot_live).reshape(
        owners_count, capacity, GTOK
    )
    send_top = (row_top.reshape(G_DEV, GTOK)[group_of] * slot_live).reshape(
        owners_count, capacity, GTOK
    )
    send_stats = jnp.stack([send_scale, send_top, send_column.astype(jnp.float32)], axis=-1)
    got_stats = lax.all_to_all(send_stats, "vocab", split_axis=0, concat_axis=0, tiled=True)
    got_scale, got_top = got_stats[..., 0], got_stats[..., 1]
    got_column = got_stats[..., 2].astype(jnp.int32)
    word_index = jnp.arange(BW, dtype=jnp.int32)
    is_target = (got_column[..., None] == word_index).astype(jnp.float32)
    live_here = got_scale[..., None] > 0
    prob_here = (
        jnp.where(live_here, jnp.exp(scores_here - got_top[..., None]) * got_scale[..., None], 0.0)
        - is_target
    ).astype(jnp.bfloat16)
    hidden_part = jnp.einsum(
        "scqw,wd->scqd", prob_here, cand_embed, preferred_element_type=jnp.float32
    ).astype(jnp.bfloat16)
    hidden_part, prob_late = lax.optimization_barrier((hidden_part, prob_freq))
    parts_home = lax.all_to_all(hidden_part, "vocab", split_axis=0, concat_axis=0, tiled=True)
    window = prob_here
    cand_partial = jnp.einsum("scqw,scqd->wd", window, got_rows, preferred_element_type=jnp.float32)
    grad_cand = lax.psum_scatter(
        cand_partial,
        "token",
        scatter_dimension=0,
        tiled=True,
    )
    part_rows = parts_home.reshape(slot_count, GTOK, D)[landing].reshape(G_DEV, K, GTOK, D)
    freq_part = jnp.dot(prob_freq, freq_table, preferred_element_type=jnp.float32)
    grad_rows = freq_part + jnp.sum(part_rows, axis=1, dtype=jnp.float32).reshape(token_total, D)
    undo = (
        jnp.zeros((token_total,), jnp.int32)
        .at[listing]
        .set(jnp.arange(token_total, dtype=jnp.int32))
    )
    position_of = (
        jnp.zeros((owners_count,), jnp.int32)
        .at[owner_order]
        .set(jnp.arange(owners_count, dtype=jnp.int32))
    )
    embed_columns = (
        position_of[:, None] * PANEL + jnp.arange(PANEL, dtype=jnp.int32)[None, :]
    ).reshape(freq_count)
    embed_columns = (
        embed_columns.reshape(freq_count // token_count, token_count).T.reshape(freq_count)
    )
    prob_embed = prob_late[:, embed_columns]
    window = prob_embed
    freq_partial = jnp.einsum("tf,td->fd", window, grouped, preferred_element_type=jnp.float32)
    freq_partial = freq_partial.reshape(token_count, freq_count // token_count, D)
    freq_partial = lax.psum_scatter(freq_partial, "token", scatter_dimension=0, tiled=True)
    grad_freq = halving_sum(freq_partial.reshape(owners_count, D), "vocab")
    logits = all_scores.astype(jnp.bfloat16)[undo]
    loss = token_loss[undo]
    grad_hidden = grad_rows.astype(jnp.bfloat16)[undo]
    return (logits, loss, grad_hidden, grad_cand, grad_freq)


def solution(mesh):
    in_specs = (
        P(("vocab", "token"), None),
        P("vocab", None),
        P("vocab", None),
        P(),
        P(("vocab", "token"), None),
        P(("vocab", "token"), None),
        P(("vocab", "token")),
    )
    out_specs = (
        P(("vocab", "token"), None),
        P(("vocab", "token")),
        P(("vocab", "token"), None),
        P(("vocab", "token"), None),
        P(("vocab", "token"), None),
    )
    return jax.shard_map(per_device_body, mesh=mesh, in_specs=in_specs, out_specs=out_specs, check_vma=False)
```

```python
import jax
import jax.numpy as jnp
from jax import lax
from jax.sharding import PartitionSpec as P

D = 4096
BW = 128
K = 4
GTOK = 8
PANEL = 4
G_DEV = 16


def halving_sum(rows, axis):
    count = lax.axis_size(axis)
    depth = count.bit_length() - 1
    me = lax.axis_index(axis)
    pieces = rows.reshape((2,) * depth + rows.shape[1:])
    bits = list(range(depth - 1, -1, -1))
    order = [0, 4, 5, 1, 2, 3] if depth == 6 else list(range(depth))
    for bit in order:
        place = bits.index(bit)
        mine = (me >> bit) & 1
        keep = lax.dynamic_index_in_dim(pieces, mine, axis=place, keepdims=False)
        give = lax.dynamic_index_in_dim(pieces, 1 - mine, axis=place, keepdims=False)
        pairs = [(i, i ^ (1 << bit)) for i in range(count)]
        pieces = keep + lax.ppermute(give, axis, pairs)
        bits.remove(bit)
    return pieces.reshape((1,) + rows.shape[1:])


def per_device_body(hidden, cand_embed, freq_embed, owner_order, cand_blocks, group_tokens, target_slot):
    owners_count = lax.axis_size("vocab")
    token_total = hidden.shape[0]
    freq_count = owners_count * PANEL
    capacity = 2 * G_DEV * K // owners_count
    slot_count = owners_count * capacity
    requests = G_DEV * K
    listing = group_tokens[0]
    grouped = hidden[listing]
    targets = target_slot[listing]
    panels = lax.all_gather(freq_embed, "vocab", axis=0, tiled=True)
    freq_table = panels.reshape(owners_count, PANEL, D)[owner_order].reshape(freq_count, D)
    owner_of = cand_blocks.reshape(requests)
    owner_hot = (owner_of[:, None] == jnp.arange(owners_count, dtype=jnp.int32)[None, :]).astype(
        jnp.int32
    )
    ranking = jnp.sum(jnp.cumsum(owner_hot, axis=0) * owner_hot, axis=1) - 1
    landing = owner_of * capacity + ranking
    placed = (landing[None, :] == jnp.arange(slot_count, dtype=jnp.int32)[:, None]).astype(
        jnp.int32
    )
    occupied = jnp.sum(placed, axis=1)
    request_of = jnp.sum(placed * jnp.arange(requests, dtype=jnp.int32)[None, :], axis=1)
    group_of = request_of // K
    block_rank = request_of % K
    send_rows = hidden[listing.reshape(G_DEV, GTOK)[group_of]].reshape(owners_count, capacity, GTOK, D)
    group_targets = targets.reshape(G_DEV, GTOK)
    column = group_targets[group_of] - freq_count - block_rank[:, None] * BW
    inside = (column >= 0) & (column < BW) & (occupied[:, None] > 0)
    send_column = jnp.where(inside, column, -1).reshape(owners_count, capacity, GTOK)
    got_rows = lax.all_to_all(send_rows, "vocab", split_axis=0, concat_axis=0, tiled=True)
    scores_here = jnp.einsum(
        "scqd,wd->scqw", got_rows, cand_embed, preferred_element_type=jnp.float32
    )
    scores_home = lax.all_to_all(scores_here, "vocab", split_axis=0, concat_axis=0, tiled=True)
    returned = scores_home.reshape(slot_count, GTOK, BW)[landing]
    cand_scores = (
        returned.reshape(G_DEV, K, GTOK, BW).transpose(0, 2, 1, 3).reshape(token_total, K * BW)
    )
    freq_scores = jnp.einsum("td,fd->tf", grouped, freq_table, preferred_element_type=jnp.float32)
    all_scores = jnp.concatenate([freq_scores, cand_scores], axis=1)
    row_top = jnp.max(all_scores, axis=1)
    exponentials = jnp.exp(all_scores - row_top[:, None])
    total = jnp.sum(exponentials, axis=1)
    inverse_total = 1.0 / total
    columns = jnp.arange(all_scores.shape[1], dtype=jnp.int32)
    target_hot = (targets[:, None] == columns[None, :]).astype(jnp.float32)
    token_loss = jnp.log(total) + row_top - jnp.sum(target_hot * all_scores, axis=1)
    prob_freq = (
        exponentials[:, :freq_count] * inverse_total[:, None] - target_hot[:, :freq_count]
    ).astype(jnp.bfloat16)
    slot_live = occupied[:, None].astype(jnp.float32)
    send_scale = (inverse_total.reshape(G_DEV, GTOK)[group_of] * slot_live).reshape(
        owners_count, capacity, GTOK
    )
    send_top = (row_top.reshape(G_DEV, GTOK)[group_of] * slot_live).reshape(
        owners_count, capacity, GTOK
    )
    send_stats = jnp.stack([send_scale, send_top, send_column.astype(jnp.float32)], axis=-1)
    got_stats = lax.all_to_all(send_stats, "vocab", split_axis=0, concat_axis=0, tiled=True)
    got_scale, got_top = got_stats[..., 0], got_stats[..., 1]
    got_column = got_stats[..., 2].astype(jnp.int32)
    word_index = jnp.arange(BW, dtype=jnp.int32)
    is_target = (got_column[..., None] == word_index).astype(jnp.float32)
    live_here = got_scale[..., None] > 0
    prob_here = (
        jnp.where(live_here, jnp.exp(scores_here - got_top[..., None]) * got_scale[..., None], 0.0)
        - is_target
    ).astype(jnp.bfloat16)
    hidden_part = jnp.einsum(
        "scqw,wd->scqd", prob_here, cand_embed, preferred_element_type=jnp.float32
    ).astype(jnp.bfloat16)
    hidden_part, prob_late = lax.optimization_barrier((hidden_part, prob_freq))
    parts_home = lax.all_to_all(hidden_part, "vocab", split_axis=0, concat_axis=0, tiled=True)
    window = prob_here
    cand_partial = jnp.einsum("scqw,scqd->wd", window, got_rows, preferred_element_type=jnp.float32)
    grad_cand = lax.psum_scatter(
        cand_partial,
        "token",
        scatter_dimension=0,
        tiled=True,
    )
    part_rows = parts_home.reshape(slot_count, GTOK, D)[landing].reshape(G_DEV, K, GTOK, D)
    freq_part = jnp.dot(prob_freq, freq_table, preferred_element_type=jnp.float32)
    grad_rows = freq_part + jnp.sum(part_rows, axis=1, dtype=jnp.float32).reshape(token_total, D)
    undo = (
        jnp.zeros((token_total,), jnp.int32)
        .at[listing]
        .set(jnp.arange(token_total, dtype=jnp.int32))
    )
    position_of = (
        jnp.zeros((owners_count,), jnp.int32)
        .at[owner_order]
        .set(jnp.arange(owners_count, dtype=jnp.int32))
    )
    embed_columns = (
        position_of[:, None] * PANEL + jnp.arange(PANEL, dtype=jnp.int32)[None, :]
    ).reshape(freq_count)
    token_count = lax.axis_size("token")
    embed_columns = (
        embed_columns.reshape(freq_count // token_count, token_count).T.reshape(freq_count)
    )
    prob_embed = prob_late[:, embed_columns]
    window = prob_embed
    freq_partial = jnp.einsum("tf,td->fd", window, grouped, preferred_element_type=jnp.float32)
    freq_partial = freq_partial.reshape(token_count, freq_count // token_count, D)
    freq_partial = lax.psum_scatter(freq_partial, "token", scatter_dimension=0, tiled=True)
    grad_freq = halving_sum(freq_partial.reshape(owners_count, D), "vocab")
    logits = all_scores.astype(jnp.bfloat16)[undo]
    loss = token_loss[undo]
    grad_hidden = grad_rows.astype(jnp.bfloat16)[undo]
    return (logits, loss, grad_hidden, grad_cand, grad_freq)


def solution(mesh):
    in_specs = (
        P(("vocab", "token"), None),
        P("vocab", None),
        P("vocab", None),
        P(),
        P(("vocab", "token"), None),
        P(("vocab", "token"), None),
        P(("vocab", "token")),
    )
    out_specs = (
        P(("vocab", "token"), None),
        P(("vocab", "token")),
        P(("vocab", "token"), None),
        P(("vocab", "token"), None),
        P(("vocab", "token"), None),
    )
    return jax.shard_map(per_device_body, mesh=mesh, in_specs=in_specs, out_specs=out_specs, check_vma=False)
```

```python
import jax
import jax.numpy as jnp
from jax import lax
from jax.sharding import PartitionSpec as P

D = 4096
BW = 128
K = 4
GTOK = 8
PANEL = 4
G_DEV = 16


def halving_sum(rows, axis):
    count = lax.axis_size(axis)
    depth = count.bit_length() - 1
    me = lax.axis_index(axis)
    pieces = rows.reshape((2,) * depth + rows.shape[1:])
    bits = list(range(depth - 1, -1, -1))
    order = [0, 4, 5, 1, 2, 3] if depth == 6 else list(range(depth))
    for bit in order:
        place = bits.index(bit)
        mine = (me >> bit) & 1
        keep = lax.dynamic_index_in_dim(pieces, mine, axis=place, keepdims=False)
        give = lax.dynamic_index_in_dim(pieces, 1 - mine, axis=place, keepdims=False)
        pairs = [(i, i ^ (1 << bit)) for i in range(count)]
        pieces = keep + lax.ppermute(give, axis, pairs)
        bits.remove(bit)
    return pieces.reshape((1,) + rows.shape[1:])


def per_device_body(hidden, cand_embed, freq_embed, owner_order, cand_blocks, group_tokens, target_slot):
    owners_count = lax.axis_size("vocab")
    token_total = hidden.shape[0]
    freq_count = owners_count * PANEL
    capacity = 2 * G_DEV * K // owners_count
    slot_count = owners_count * capacity
    requests = G_DEV * K
    listing = group_tokens[0]
    grouped = hidden[listing]
    targets = target_slot[listing]
    panels = lax.all_gather(freq_embed, "vocab", axis=0, tiled=True)
    freq_table = panels.reshape(owners_count, PANEL, D)[owner_order].reshape(freq_count, D)
    owner_of = cand_blocks.reshape(requests)
    owner_hot = (owner_of[:, None] == jnp.arange(owners_count, dtype=jnp.int32)[None, :]).astype(
        jnp.int32
    )
    ranking = jnp.sum(jnp.cumsum(owner_hot, axis=0) * owner_hot, axis=1) - 1
    landing = owner_of * capacity + ranking
    placed = (landing[None, :] == jnp.arange(slot_count, dtype=jnp.int32)[:, None]).astype(
        jnp.int32
    )
    occupied = jnp.sum(placed, axis=1)
    request_of = jnp.sum(placed * jnp.arange(requests, dtype=jnp.int32)[None, :], axis=1)
    group_of = request_of // K
    block_rank = request_of % K
    send_rows = hidden[listing.reshape(G_DEV, GTOK)[group_of]].reshape(owners_count, capacity, GTOK, D)
    group_targets = targets.reshape(G_DEV, GTOK)
    column = group_targets[group_of] - freq_count - block_rank[:, None] * BW
    inside = (column >= 0) & (column < BW) & (occupied[:, None] > 0)
    send_column = jnp.where(inside, column, -1).reshape(owners_count, capacity, GTOK)
    got_rows = lax.all_to_all(send_rows, "vocab", split_axis=0, concat_axis=0, tiled=True)
    scores_here = jnp.einsum(
        "scqd,wd->scqw", got_rows, cand_embed, preferred_element_type=jnp.float32
    )
    scores_home = lax.all_to_all(scores_here, "vocab", split_axis=0, concat_axis=0, tiled=True)
    returned = scores_home.reshape(slot_count, GTOK, BW)[landing]
    cand_scores = (
        returned.reshape(G_DEV, K, GTOK, BW).transpose(0, 2, 1, 3).reshape(token_total, K * BW)
    )
    freq_scores = jnp.einsum("td,fd->tf", grouped, freq_table, preferred_element_type=jnp.float32)
    all_scores = jnp.concatenate([freq_scores, cand_scores], axis=1)
    row_top = jnp.max(all_scores, axis=1)
    exponentials = jnp.exp(all_scores - row_top[:, None])
    total = jnp.sum(exponentials, axis=1)
    inverse_total = 1.0 / total
    columns = jnp.arange(all_scores.shape[1], dtype=jnp.int32)
    target_hot = (targets[:, None] == columns[None, :]).astype(jnp.float32)
    token_loss = jnp.log(total) + row_top - jnp.sum(target_hot * all_scores, axis=1)
    prob_freq = (
        exponentials[:, :freq_count] * inverse_total[:, None] - target_hot[:, :freq_count]
    ).astype(jnp.bfloat16)
    slot_live = occupied[:, None].astype(jnp.float32)
    send_scale = (inverse_total.reshape(G_DEV, GTOK)[group_of] * slot_live).reshape(
        owners_count, capacity, GTOK
    )
    send_top = (row_top.reshape(G_DEV, GTOK)[group_of] * slot_live).reshape(
        owners_count, capacity, GTOK
    )
    send_stats = jnp.stack([send_scale, send_top, send_column.astype(jnp.float32)], axis=-1)
    got_stats = lax.all_to_all(send_stats, "vocab", split_axis=0, concat_axis=0, tiled=True)
    got_scale, got_top = got_stats[..., 0], got_stats[..., 1]
    got_column = got_stats[..., 2].astype(jnp.int32)
    word_index = jnp.arange(BW, dtype=jnp.int32)
    is_target = (got_column[..., None] == word_index).astype(jnp.float32)
    live_here = got_scale[..., None] > 0
    prob_here = (
        jnp.where(live_here, jnp.exp(scores_here - got_top[..., None]) * got_scale[..., None], 0.0)
        - is_target
    ).astype(jnp.bfloat16)
    hidden_part = jnp.einsum(
        "scqw,wd->scqd", prob_here, cand_embed, preferred_element_type=jnp.float32
    ).astype(jnp.bfloat16)
    hidden_part, prob_late = lax.optimization_barrier((hidden_part, prob_freq))
    parts_home = lax.all_to_all(hidden_part, "vocab", split_axis=0, concat_axis=0, tiled=True)
    window = prob_here
    cand_partial = jnp.einsum("scqw,scqd->wd", window, got_rows, preferred_element_type=jnp.float32)
    grad_cand = lax.psum_scatter(
        cand_partial,
        "token",
        scatter_dimension=0,
        tiled=True,
    )
    undo = (
        jnp.zeros((token_total,), jnp.int32)
        .at[listing]
        .set(jnp.arange(token_total, dtype=jnp.int32))
    )
    flat_index = landing.reshape(G_DEV, K)[undo // GTOK] * GTOK + (undo % GTOK)[:, None]
    slot_rows = jnp.arange(slot_count * GTOK, dtype=jnp.int32)
    select = jnp.sum((flat_index[:, :, None] == slot_rows).astype(jnp.bfloat16), axis=1)
    freq_part = jnp.dot(prob_late[undo], freq_table, preferred_element_type=jnp.float32)
    parts_flat = parts_home.reshape(slot_count * GTOK, D)
    grad_rows = freq_part + jnp.dot(select, parts_flat, preferred_element_type=jnp.float32)
    position_of = (
        jnp.zeros((owners_count,), jnp.int32)
        .at[owner_order]
        .set(jnp.arange(owners_count, dtype=jnp.int32))
    )
    embed_columns = (
        position_of[:, None] * PANEL + jnp.arange(PANEL, dtype=jnp.int32)[None, :]
    ).reshape(freq_count)
    token_count = lax.axis_size("token")
    embed_columns = (
        embed_columns.reshape(freq_count // token_count, token_count).T.reshape(freq_count)
    )
    prob_embed = prob_late[:, embed_columns]
    window = prob_embed
    freq_partial = jnp.einsum("tf,td->fd", window, grouped, preferred_element_type=jnp.float32)
    freq_partial = freq_partial.reshape(token_count, freq_count // token_count, D)
    freq_partial = lax.psum_scatter(freq_partial, "token", scatter_dimension=0, tiled=True)
    grad_freq = halving_sum(freq_partial.reshape(owners_count, D), "vocab")
    logits = all_scores.astype(jnp.bfloat16)[undo]
    loss = token_loss[undo]
    grad_hidden = grad_rows.astype(jnp.bfloat16)
    return (logits, loss, grad_hidden, grad_cand, grad_freq)


def solution(mesh):
    in_specs = (
        P(("vocab", "token"), None),
        P("vocab", None),
        P("vocab", None),
        P(),
        P(("vocab", "token"), None),
        P(("vocab", "token"), None),
        P(("vocab", "token")),
    )
    out_specs = (
        P(("vocab", "token"), None),
        P(("vocab", "token")),
        P(("vocab", "token"), None),
        P(("vocab", "token"), None),
        P(("vocab", "token"), None),
    )
    return jax.shard_map(per_device_body, mesh=mesh, in_specs=in_specs, out_specs=out_specs, check_vma=False)
```
